256 devices in a mesh: space: 32 (over x, z), member: 4 (over y), lag: 2 (over core).
Axes of the slice: x: 4, y: 4, z: 8, core: 2. Of those that a mesh axis runs over, the one named last changes fastest.
Arguments:
- anomalies: bfloat16 [2, 131072, 512], P('lag', 'space', 'member'), may hold values from -6 to 6
- mean_state: float32 [2, 131072], P('lag', 'space'), may hold values from -6 to 6
- footprints: bfloat16 [4, 2, 128, 256, 512], P(None, 'lag', 'space'), may hold values from -0.03125 to 0.03125
- slot_tiles: int32 [4, 2, 128], P(None, 'lag', 'space'), may hold values from 0 to 7, as said below
- slot_counts: int32 [4, 2, 32], P(None, 'lag', 'space'), may hold values from 0 to 4, as said below
- obs_values: float32 [32, 4, 256], P('space'), may hold values from -6 to 6
- obs_errors: float32 [32, 4, 256], P('space'), may hold values from 0.5 to 1.5
- owners: int32 [4], replicated, may hold values from 0 to 31
- batch_order: int32 [4], replicated, may hold values from 0 to 3, as said below
Outputs:
- analysis_anoms: bfloat16 [2, 131072, 512], P('lag', 'space', 'member')
- analysis_mean: float32 [2, 131072], P('lag', 'space')
The draws below stay inside these ranges and needn't reach their ends.
Inputs may be any that keep to these rules, and one draw needn't show every extreme that they name: `slot_counts`: in every batch some lag week and space group has exactly 4 live slots. `slot_tiles`: within one batch, lag week and space group the 4 slots name distinct local tiles. `batch_order`: A permutation.
All inputs are finite; a program needn't handle non-finite values.
Results may differ from the reference program's by a relative error of at most 0.008.
Values may be sent and summed in bfloat16 or wider, within the bound.
No kernel may reach another device: no remote copies, remote signals or barrier semaphores. Data moves between devices by JAX's collectives and lax.ppermute only.
A program may use at most 64 MiB of HBM per device.

```python
import math
import jax
import jax.numpy as jnp
from jax import lax

M = 512
P_SIZE = 256
TILE = 512
SLOT_DEV = 4
NB = 4
TILE_DEV = 8
LAGS = 2
CELLS = 131072
SLOTS = 128
N_SPACE = 32


def draw_slot_counts(key, part):
    key_one, key_two, key_three = jax.random.split(key, 3)
    first = jax.random.randint(key_one, (NB, LAGS, N_SPACE), 0, SLOT_DEV + 1)
    second = jax.random.randint(key_two, (NB, LAGS, N_SPACE), 0, SLOT_DEV + 1)
    counts = jnp.minimum(first, second)
    chosen = jax.random.randint(key_three, (NB, 1, 1), 0, LAGS * N_SPACE)
    position = jnp.arange(LAGS * N_SPACE).reshape(1, LAGS, N_SPACE)
    return jnp.where(position == chosen, SLOT_DEV, counts).astype(jnp.int32)


def draw_slot_tiles(key, part):
    scores = jax.random.randint(key, (NB, LAGS, N_SPACE, TILE_DEV), 0, 2 ** 20) * TILE_DEV + jnp.arange(TILE_DEV)
    ranked = jnp.argsort(scores, axis=-1, stable=True)[..., :SLOT_DEV]
    return ranked.reshape(NB, LAGS, N_SPACE * SLOT_DEV).astype(jnp.int32)


def draw_batch_order(key, part):
    order_key = jax.random.fold_in(key, 7919)
    scores = jax.random.randint(order_key, (NB,), 0, 2 ** 20) * NB + jnp.arange(NB)
    return jnp.argsort(scores, stable=True).astype(jnp.int32)


def with_ends(drawn, stream_key, smallest, top_value):
    index_at = [jax.random.randint(jax.random.fold_in(stream_key, axis), (), 0, length) for axis, length in enumerate(drawn.shape)]
    main_axis = drawn.shape.index(max(drawn.shape))
    next_to = index_at[:main_axis] + [(index_at[main_axis] + 1) % drawn.shape[main_axis]] + index_at[main_axis + 1:]
    return drawn.at[tuple(index_at)].set(smallest).at[tuple(next_to)].set(top_value)


def shard_levels(rng, extent, shards, least, largest):
    gain, own = 1.0, jax.random.fold_in(rng, 6)
    for dim, blocks in shards:
        draws = jnp.exp(jax.random.uniform(jax.random.fold_in(own, dim), (blocks,), jnp.float32, least / len(shards), largest / len(shards)))
        gain = gain * jnp.repeat(draws, extent[dim] // blocks).reshape([-1 if axis == dim else 1 for axis in range(len(extent))])
    return gain


def bell_draw(own_key, dims, spread, most, pieces=(), kind=jnp.bfloat16):
    gain = shard_levels(own_key, dims, pieces, -0.22, 0.18) if pieces else 1.0
    entries = jax.random.normal(own_key, dims, jnp.float32) * spread * gain
    return jnp.minimum(jnp.maximum(entries, -most), most).astype(kind)


def setup_inputs(seed: int = 0) -> dict:
    splits = jax.random.split(jax.random.key(seed), 10)
    anomalies = bell_draw(splits[0], (LAGS, CELLS, M), 1.0, 6.0, ((0, 2), (1, 32), (2, 4)))
    mean_state = bell_draw(splits[1], (LAGS, CELLS), 1.0, 6.0, ((0, 2), (1, 32)), jnp.float32)
    footprints = bell_draw(splits[2], (NB, LAGS, SLOTS, P_SIZE, TILE), (TILE * SLOTS * LAGS // 4) ** -0.5, 0.03125, ((1, 2), (2, 32)))
    slot_tiles = draw_slot_tiles(jax.random.fold_in(splits[9], 71), 0)
    slot_counts = draw_slot_counts(jax.random.fold_in(splits[9], 71), 0)
    obs_values = bell_draw(splits[5], (N_SPACE, NB, P_SIZE), 1.0, 6.0, ((0, 32),), jnp.float32)
    obs_errors = jnp.clip(jnp.exp(math.log(1.5) - 1.0986123 * jax.random.uniform(splits[6], (N_SPACE, NB, P_SIZE), jnp.float32) ** shard_levels(splits[6], (N_SPACE, NB, P_SIZE), ((0, 32),), -0.2, 0.2)), 0.5, 1.5)
    owners = with_ends(jax.random.randint(splits[7], (NB,), 0, N_SPACE), jax.random.fold_in(splits[7], 1), 0, N_SPACE - 1).astype(jnp.int32)
    batch_order = draw_batch_order(jax.random.fold_in(splits[9], 71), 0)
    return {"anomalies": anomalies, "mean_state": mean_state, "footprints": footprints, "slot_tiles": slot_tiles, "slot_counts": slot_counts, "obs_values": obs_values, "obs_errors": obs_errors, "owners": owners, "batch_order": batch_order}


def innovation(obs_round, values_now, obs_means, errors_now, members):
    obs_total = obs_round.shape[0]
    innov_cov = jnp.dot(obs_round.astype(jnp.float32), obs_round.T.astype(jnp.float32), preferred_element_type=jnp.float32) / (members - 1) + jnp.diag(errors_now * errors_now)
    factor = jnp.linalg.cholesky(innov_cov)
    identity = jnp.eye(obs_total, dtype=jnp.float32)
    inverse_sum = lax.linalg.triangular_solve(factor + jnp.diag(errors_now), identity, left_side=True, lower=True)
    transform = lax.linalg.triangular_solve(factor, inverse_sum, left_side=True, lower=True, transpose_a=True)
    forward = lax.linalg.triangular_solve(factor, (values_now - obs_means)[:, None], left_side=True, lower=True)
    weights_obs = lax.linalg.triangular_solve(factor, forward, left_side=True, lower=True, transpose_a=True)[:, 0]
    return (transform, weights_obs)

def reference(anomalies, mean_state, footprints, slot_tiles, slot_counts, obs_values, obs_errors, owners, batch_order):
    highest = lax.Precision.HIGHEST
    tile_total = N_SPACE * TILE_DEV
    tile_anoms = anomalies.reshape(LAGS, tile_total, TILE, M)
    tile_means = mean_state.reshape(LAGS, tile_total, TILE)
    slot_group = (jnp.arange(SLOTS) // SLOT_DEV).astype(jnp.int32)
    slot_place = (jnp.arange(SLOTS) % SLOT_DEV).astype(jnp.int32)
    lag_ids = jnp.arange(LAGS).astype(jnp.int32)[:, None]
    for position in range(NB):
        batch_now = batch_order[position]
        values_now = obs_values[owners[batch_now], batch_now]
        errors_now = obs_errors[owners[batch_now], batch_now]
        global_ids = slot_group[None, :] * TILE_DEV + slot_tiles[batch_now]
        live_mask = slot_place[None, :] < slot_counts[batch_now][:, slot_group]
        slot_anoms = tile_anoms[lag_ids, global_ids]
        slot_means = tile_means[lag_ids, global_ids]
        prints = footprints[batch_now].astype(jnp.float32)
        masked = jnp.where(live_mask[:, :, None, None], slot_anoms, 0).astype(jnp.float32)
        obs_anoms = jnp.einsum('lspt,lstm->pm', prints, masked)
        mean_round = jnp.where(live_mask[:, :, None], slot_means.astype(jnp.bfloat16), 0).astype(jnp.float32)
        obs_means = jnp.einsum('lspt,lst->p', prints, mean_round)
        obs_round = obs_anoms.astype(jnp.bfloat16)
        transform, weights_obs = innovation(obs_round, values_now, obs_means, errors_now, M)
        wide_anoms = slot_anoms.astype(jnp.float32)
        wide_obs = obs_round.astype(jnp.float32)
        covariance = jnp.einsum('lstm,pm->lstp', wide_anoms, wide_obs)
        gain_tile = (jnp.einsum('lstp,pq->lstq', covariance, transform, precision=highest) / (M - 1)).astype(jnp.bfloat16)
        updated = (wide_anoms - jnp.einsum('lstp,pm->lstm', gain_tile.astype(jnp.float32), wide_obs)).astype(jnp.bfloat16)
        tile_anoms = tile_anoms.at[lag_ids, global_ids].set(jnp.where(live_mask[:, :, None, None], updated, slot_anoms))
        shifted = slot_means + jnp.einsum('lstp,p->lst', covariance, weights_obs, precision=highest) / (M - 1)
        tile_means = tile_means.at[lag_ids, global_ids].set(jnp.where(live_mask[:, :, None], shifted, slot_means))
    return (tile_anoms.reshape(LAGS, CELLS, M), tile_means.reshape(LAGS, CELLS))
```

```python
import jax
import jax.numpy as jnp
from jax import lax
from jax.sharding import PartitionSpec as P


def spread(array, axis, root):
    mine = lax.axis_index(axis) == root
    return lax.psum(jnp.where(mine, array, jnp.zeros_like(array)), axis)


def innovation(obs_round, values_now, obs_means, errors_now, members):
    obs_total = obs_round.shape[0]
    innov_cov = jnp.dot(obs_round, obs_round.T, preferred_element_type=jnp.float32) / (
        members - 1
    ) + jnp.diag(errors_now * errors_now)
    factor = jnp.linalg.cholesky(innov_cov)
    identity = jnp.eye(obs_total, dtype=jnp.float32)
    inverse_sum = lax.linalg.triangular_solve(
        factor + jnp.diag(errors_now), identity, left_side=True, lower=True
    )
    transform = lax.linalg.triangular_solve(
        factor, inverse_sum, left_side=True, lower=True, transpose_a=True
    )
    forward = lax.linalg.triangular_solve(
        factor, (values_now - obs_means)[:, None], left_side=True, lower=True
    )
    weights_obs = lax.linalg.triangular_solve(
        factor, forward, left_side=True, lower=True, transpose_a=True
    )[:, 0]
    return (transform, weights_obs)


def body(
    anomalies,
    mean_state,
    footprints,
    slot_tiles,
    slot_counts,
    obs_values,
    obs_errors,
    owners,
    batch_order,
):
    highest = lax.Precision.HIGHEST
    batches = footprints.shape[0]
    slot_dev = footprints.shape[2]
    tile_cells = footprints.shape[4]
    member_dev = anomalies.shape[2]
    groups = lax.axis_size("member")
    members = member_dev * groups
    tile_anoms = anomalies[0].reshape(-1, tile_cells, member_dev)
    tile_means = mean_state[0].reshape(-1, tile_cells)
    me_member = lax.axis_index("member")
    me_space = lax.axis_index("space")
    me_lag = lax.axis_index("lag")
    lead = (me_member == 0) & (me_lag == 0)
    for position in range(batches):
        batch_now = batch_order[position]
        owner_here = lead & (me_space == owners[batch_now])
        own_values = jnp.where(owner_here, obs_values[0, batch_now], 0)
        own_errors = jnp.where(owner_here, obs_errors[0, batch_now], 0)
        tile_ids = slot_tiles[batch_now, 0]
        live_count = slot_counts[batch_now, 0, 0]
        live_mask = jnp.arange(slot_dev) < live_count
        slot_anoms = tile_anoms[tile_ids]
        slot_means = tile_means[tile_ids]
        prints = footprints[batch_now, 0]
        mean_round = slot_means.astype(jnp.bfloat16)
        masked = jnp.where(live_mask[:, None, None], slot_anoms, 0)
        part_anoms = jnp.einsum("spt,stm->pm", prints, masked, preferred_element_type=jnp.float32)
        masked_mean = jnp.where(live_mask[:, None], mean_round, 0)
        part_means = jnp.einsum(
            "spt,st->p", prints, masked_mean, preferred_element_type=jnp.float32
        )
        slotted = jnp.zeros((groups,) + part_anoms.shape, jnp.float32)
        slotted = lax.dynamic_update_index_in_dim(slotted, part_anoms, me_member, 0)
        part_means = jnp.where(me_member == 0, part_means, 0)
        all_anoms_obs, obs_means, values_now, errors_now = lax.psum(
            (slotted, part_means, own_values, own_errors), ("space", "member", "lag")
        )
        all_round = all_anoms_obs.astype(jnp.bfloat16)
        own_round = lax.dynamic_index_in_dim(all_round, me_member, 0, keepdims=False)
        obs_round = jnp.transpose(all_round, (1, 0, 2)).reshape(all_round.shape[1], -1)
        transform, weights_obs = innovation(obs_round, values_now, obs_means, errors_now, members)
        all_anoms = lax.all_gather(slot_anoms, "member", axis=2, tiled=True)
        covariance = jnp.einsum(
            "stm,pm->stp", all_anoms, obs_round, preferred_element_type=jnp.float32
        )
        gain_tile = (
            jnp.einsum("stp,pq->stq", covariance, transform, precision=highest) / (members - 1)
        ).astype(jnp.bfloat16)
        shift_mean = jnp.einsum("stp,p->st", covariance, weights_obs, precision=highest) / (
            members - 1
        )
        step_anoms = jnp.einsum(
            "stp,pm->stm", gain_tile, own_round, preferred_element_type=jnp.float32
        )
        updated = (slot_anoms.astype(jnp.float32) - step_anoms).astype(jnp.bfloat16)
        tile_anoms = tile_anoms.at[tile_ids].set(
            jnp.where(live_mask[:, None, None], updated, slot_anoms)
        )
        tile_means = tile_means.at[tile_ids].set(
            jnp.where(live_mask[:, None], slot_means + shift_mean, slot_means)
        )
    return (tile_anoms.reshape(1, -1, member_dev), tile_means.reshape(1, -1))


def solution(mesh):
    return jax.shard_map(
        body,
        mesh=mesh,
        in_specs=(
            P("lag", "space", "member"),
            P("lag", "space"),
            P(None, "lag", "space", None, None),
            P(None, "lag", "space"),
            P(None, "lag", "space"),
            P("space", None, None),
            P("space", None, None),
            P(),
            P(),
        ),
        out_specs=(P("lag", "space", "member"), P("lag", "space")),
        check_vma=False,
    )
```

```python
import jax
import jax.numpy as jnp
from jax import lax
from jax.sharding import PartitionSpec as P


def spread(array, axis, root):
    mine = lax.axis_index(axis) == root
    return lax.psum(jnp.where(mine, array, jnp.zeros_like(array)), axis)


def innovation(obs_round, values_now, obs_means, errors_now, members):
    highest = lax.Precision.HIGHEST
    obs_total = obs_round.shape[0]
    half = obs_total // 2
    innov_cov = jnp.dot(obs_round, obs_round.T, preferred_element_type=jnp.float32) / (
        members - 1
    ) + jnp.diag(errors_now * errors_now)
    innov_cov = (innov_cov + innov_cov.T) * 0.5
    eye = jnp.eye(half, dtype=jnp.float32)
    eyes = jnp.stack([eye, eye])
    errors_top, errors_low = errors_now[:half], errors_now[half:]
    factor_11 = lax.linalg.cholesky(innov_cov[:half, :half], symmetrize_input=False)
    inv_top = lax.linalg.triangular_solve(
        jnp.stack([factor_11, factor_11 + jnp.diag(errors_top)]), eyes, left_side=True, lower=True
    )
    factor_11_inv, sum_11_inv = inv_top[0], inv_top[1]
    factor_21 = jnp.dot(innov_cov[half:, :half], factor_11_inv.T, precision=highest)
    schur = innov_cov[half:, half:] - jnp.dot(factor_21, factor_21.T, precision=highest)
    factor_22 = lax.linalg.cholesky(schur, symmetrize_input=True)
    inv_low = lax.linalg.triangular_solve(
        jnp.stack([factor_22, factor_22 + jnp.diag(errors_low)]), eyes, left_side=True, lower=True
    )
    factor_22_inv, sum_22_inv = inv_low[0], inv_low[1]
    factor_21_inv = -jnp.dot(
        factor_22_inv, jnp.dot(factor_21, factor_11_inv, precision=highest), precision=highest
    )
    sum_21_inv = -jnp.dot(
        sum_22_inv, jnp.dot(factor_21, sum_11_inv, precision=highest), precision=highest
    )
    zeros = jnp.zeros((half, half), jnp.float32)
    factor_inv = jnp.block([[factor_11_inv, zeros], [factor_21_inv, factor_22_inv]])
    inverse_sum = jnp.block([[sum_11_inv, zeros], [sum_21_inv, sum_22_inv]])
    transform = jnp.dot(factor_inv.T, inverse_sum, precision=highest)
    forward = jnp.dot(factor_inv, values_now - obs_means, precision=highest)
    weights_obs = jnp.dot(factor_inv.T, forward, precision=highest)
    return (transform, weights_obs)


def body(
    anomalies,
    mean_state,
    footprints,
    slot_tiles,
    slot_counts,
    obs_values,
    obs_errors,
    owners,
    batch_order,
):
    highest = lax.Precision.HIGHEST
    batches = footprints.shape[0]
    slot_dev = footprints.shape[2]
    tile_cells = footprints.shape[4]
    member_dev = anomalies.shape[2]
    groups = lax.axis_size("member")
    members = member_dev * groups
    tile_anoms = anomalies[0].reshape(-1, tile_cells, member_dev)
    tile_means = mean_state[0].reshape(-1, tile_cells)
    me_member = lax.axis_index("member")
    me_space = lax.axis_index("space")
    me_lag = lax.axis_index("lag")
    lead = (me_member == 0) & (me_lag == 0)
    for position in range(batches):
        batch_now = batch_order[position]
        owner_here = lead & (me_space == owners[batch_now])
        own_values = jnp.where(owner_here, obs_values[0, batch_now], 0)
        own_errors = jnp.where(owner_here, obs_errors[0, batch_now], 0)
        tile_ids = slot_tiles[batch_now, 0]
        live_count = slot_counts[batch_now, 0, 0]
        live_mask = jnp.arange(slot_dev) < live_count
        slot_anoms = tile_anoms[tile_ids]
        slot_means = tile_means[tile_ids]
        prints = footprints[batch_now, 0]
        mean_round = slot_means.astype(jnp.bfloat16)
        masked = jnp.where(live_mask[:, None, None], slot_anoms, 0)
        part_anoms = jnp.einsum("spt,stm->pm", prints, masked, preferred_element_type=jnp.float32)
        masked_mean = jnp.where(live_mask[:, None], mean_round, 0)
        part_means = jnp.einsum(
            "spt,st->p", prints, masked_mean, preferred_element_type=jnp.float32
        )
        slotted = jnp.zeros((groups,) + part_anoms.shape, jnp.float32)
        slotted = lax.dynamic_update_index_in_dim(slotted, part_anoms, me_member, 0)
        part_means = jnp.where(me_member == 0, part_means, 0)
        all_anoms_obs, obs_means, values_now, errors_now = lax.psum(
            (slotted, part_means, own_values, own_errors), ("space", "member", "lag")
        )
        all_round = all_anoms_obs.astype(jnp.bfloat16)
        own_round = lax.dynamic_index_in_dim(all_round, me_member, 0, keepdims=False)
        obs_round = jnp.transpose(all_round, (1, 0, 2)).reshape(all_round.shape[1], -1)
        transform, weights_obs = innovation(obs_round, values_now, obs_means, errors_now, members)
        all_anoms = lax.all_gather(slot_anoms, "member", axis=2, tiled=True)
        covariance = jnp.einsum(
            "stm,pm->stp", all_anoms, obs_round, preferred_element_type=jnp.float32
        )
        gain_tile = (
            jnp.einsum("stp,pq->stq", covariance, transform, precision=highest) / (members - 1)
        ).astype(jnp.bfloat16)
        shift_mean = jnp.einsum("stp,p->st", covariance, weights_obs, precision=highest) / (
            members - 1
        )
        step_anoms = jnp.einsum(
            "stp,pm->stm", gain_tile, own_round, preferred_element_type=jnp.float32
        )
        updated = (slot_anoms.astype(jnp.float32) - step_anoms).astype(jnp.bfloat16)
        tile_anoms = tile_anoms.at[tile_ids].set(
            jnp.where(live_mask[:, None, None], updated, slot_anoms)
        )
        tile_means = tile_means.at[tile_ids].set(
            jnp.where(live_mask[:, None], slot_means + shift_mean, slot_means)
        )
    return (tile_anoms.reshape(1, -1, member_dev), tile_means.reshape(1, -1))


def solution(mesh):
    return jax.shard_map(
        body,
        mesh=mesh,
        in_specs=(
            P("lag", "space", "member"),
            P("lag", "space"),
            P(None, "lag", "space", None, None),
            P(None, "lag", "space"),
            P(None, "lag", "space"),
            P("space", None, None),
            P("space", None, None),
            P(),
            P(),
        ),
        out_specs=(P("lag", "space", "member"), P("lag", "space")),
        check_vma=False,
    )
```

```python
import jax
import jax.numpy as jnp
from jax import lax
from jax.sharding import PartitionSpec as P


def spread(array, axis, root):
    mine = lax.axis_index(axis) == root
    return lax.psum(jnp.where(mine, array, jnp.zeros_like(array)), axis)


def innovation(obs_round, values_now, obs_means, errors_now, members):
    highest = lax.Precision.HIGHEST
    obs_total = obs_round.shape[0]
    half = obs_total // 2
    innov_cov = jnp.dot(obs_round, obs_round.T, preferred_element_type=jnp.float32) / (
        members - 1
    ) + jnp.diag(errors_now * errors_now)
    innov_cov = (innov_cov + innov_cov.T) * 0.5
    eye = jnp.eye(half, dtype=jnp.float32)
    eyes = jnp.stack([eye, eye])
    errors_top, errors_low = errors_now[:half], errors_now[half:]
    factor_11 = lax.linalg.cholesky(innov_cov[:half, :half], symmetrize_input=False)
    inv_top = lax.linalg.triangular_solve(
        jnp.stack([factor_11, factor_11 + jnp.diag(errors_top)]), eyes, left_side=True, lower=True
    )
    factor_11_inv, sum_11_inv = inv_top[0], inv_top[1]
    factor_21 = jnp.dot(innov_cov[half:, :half], factor_11_inv.T, precision=highest)
    schur = innov_cov[half:, half:] - jnp.dot(factor_21, factor_21.T, precision=highest)
    factor_22 = lax.linalg.cholesky(schur, symmetrize_input=True)
    inv_low = lax.linalg.triangular_solve(
        jnp.stack([factor_22, factor_22 + jnp.diag(errors_low)]), eyes, left_side=True, lower=True
    )
    factor_22_inv, sum_22_inv = inv_low[0], inv_low[1]
    factor_21_inv = -jnp.dot(
        factor_22_inv, jnp.dot(factor_21, factor_11_inv, precision=highest), precision=highest
    )
    sum_21_inv = -jnp.dot(
        sum_22_inv, jnp.dot(factor_21, sum_11_inv, precision=highest), precision=highest
    )
    zeros = jnp.zeros((half, half), jnp.float32)
    factor_inv = jnp.block([[factor_11_inv, zeros], [factor_21_inv, factor_22_inv]])
    inverse_sum = jnp.block([[sum_11_inv, zeros], [sum_21_inv, sum_22_inv]])
    transform = jnp.dot(factor_inv.T, inverse_sum, precision=highest)
    forward = jnp.dot(factor_inv, values_now - obs_means, precision=highest)
    weights_obs = jnp.dot(factor_inv.T, forward, precision=highest)
    return (transform, weights_obs)


def body(
    anomalies,
    mean_state,
    footprints,
    slot_tiles,
    slot_counts,
    obs_values,
    obs_errors,
    owners,
    batch_order,
):
    highest = lax.Precision.HIGHEST
    batches = footprints.shape[0]
    slot_dev = footprints.shape[2]
    tile_cells = footprints.shape[4]
    member_dev = anomalies.shape[2]
    groups = lax.axis_size("member")
    members = member_dev * groups
    me_member = lax.axis_index("member")
    me_space = lax.axis_index("space")
    me_lag = lax.axis_index("lag")
    lead = (me_member == 0) & (me_lag == 0)
    tile_anoms = anomalies[0].reshape(-1, tile_cells, member_dev)
    tile_means = mean_state[0].reshape(-1, tile_cells)
    tiles_dev = tile_anoms.shape[0]
    all_tiles = lax.all_gather(tile_anoms, "member", axis=2, tiled=True)
    local_ids = jnp.arange(tiles_dev, dtype=jnp.int32)
    slot_place = jnp.arange(slot_dev, dtype=jnp.int32)
    pattern = jnp.zeros((tiles_dev,), jnp.int32)
    pieces, mean_parts, value_parts, error_parts = [], [], [], []
    for position in range(batches):
        batch_now = batch_order[position]
        tile_ids = slot_tiles[batch_now, 0]
        live_slot = slot_place < slot_counts[batch_now, 0, 0]
        prints = footprints[batch_now, 0]
        slot_anoms = tile_anoms[tile_ids]
        slot_means = tile_means[tile_ids].astype(jnp.float32)
        proj = jnp.einsum("spt,stm->spm", prints, slot_anoms, preferred_element_type=jnp.float32)
        n_pat = 2**position
        select = live_slot[:, None] & (
            pattern[tile_ids][:, None] == jnp.arange(n_pat, dtype=jnp.int32)[None, :]
        )
        pieces.append(jnp.sum(jnp.where(select[:, :, None, None], proj[:, None], 0.0), axis=0))
        masked_mean = jnp.where(live_slot[:, None], slot_means, 0.0)
        mean_parts.append(
            jnp.einsum("spt,st->p", prints.astype(jnp.float32), masked_mean, precision=highest)
        )
        owner_here = lead & (me_space == owners[batch_now])
        value_parts.append(jnp.where(owner_here, obs_values[0, batch_now], 0.0))
        error_parts.append(jnp.where(owner_here, obs_errors[0, batch_now], 0.0))
        live_tile = jnp.any((tile_ids[:, None] == local_ids[None, :]) & live_slot[:, None], axis=0)
        pattern = pattern + jnp.where(live_tile, 1 << position, 0)
    projected = jnp.concatenate(pieces, axis=0)
    slotted = jnp.zeros((projected.shape[0], groups) + projected.shape[1:], jnp.float32)
    slotted = lax.dynamic_update_index_in_dim(slotted, projected, me_member, 1)
    mean_parts = jnp.where(me_member == 0, jnp.stack(mean_parts), 0.0)
    summed, obs_means_base, values_all, errors_all = lax.psum(
        (slotted, mean_parts, jnp.stack(value_parts), jnp.stack(error_parts)),
        ("space", "member", "lag"),
    )
    summed = summed.astype(jnp.bfloat16)
    summed = jnp.transpose(summed, (0, 2, 1, 3)).reshape(summed.shape[0], summed.shape[2], members)
    transforms = [jnp.eye(members, dtype=jnp.float32)]
    shifts = [jnp.zeros((members,), jnp.float32)]
    offset = 0
    for position in range(batches):
        n_pat = 2**position
        part = summed[offset : offset + n_pat].astype(jnp.float32)
        offset += n_pat
        obs_anoms = jnp.einsum("spm,smn->pn", part, jnp.stack(transforms), precision=highest)
        obs_means = obs_means_base[position] + jnp.einsum(
            "spm,sm->p", part, jnp.stack(shifts), precision=highest
        )
        obs_round = obs_anoms.astype(jnp.bfloat16)
        transform, weights_obs = innovation(
            obs_round, values_all[position], obs_means, errors_all[position], members
        )
        wide_obs = obs_round.astype(jnp.float32)
        step = jnp.dot(
            wide_obs.T, jnp.dot(transform, wide_obs, precision=highest), precision=highest
        ) / (members - 1)
        lift = jnp.dot(wide_obs.T, weights_obs, precision=highest) / (members - 1)
        new_transforms = [t - jnp.dot(t, step, precision=highest) for t in transforms]
        new_shifts = [s + jnp.dot(t, lift, precision=highest) for t, s in zip(transforms, shifts)]
        transforms = transforms + new_transforms
        shifts = shifts + new_shifts
    own_cols = lax.dynamic_slice_in_dim(
        jnp.stack(transforms), me_member * member_dev, member_dev, axis=2
    )
    tile_transform = own_cols[pattern]
    tile_shift = jnp.stack(shifts)[pattern]
    wide_tiles = all_tiles.astype(jnp.float32)
    updated = jnp.einsum("tcm,tmn->tcn", wide_tiles, tile_transform, precision=highest)
    touched = pattern > 0
    new_anoms = jnp.where(touched[:, None, None], updated.astype(jnp.bfloat16), tile_anoms)
    shift_mean = jnp.einsum("tcm,tm->tc", wide_tiles, tile_shift, precision=highest)
    new_means = jnp.where(touched[:, None], tile_means + shift_mean, tile_means)
    return (new_anoms.reshape(1, -1, member_dev), new_means.reshape(1, -1))


def solution(mesh):
    return jax.shard_map(
        body,
        mesh=mesh,
        in_specs=(
            P("lag", "space", "member"),
            P("lag", "space"),
            P(None, "lag", "space", None, None),
            P(None, "lag", "space"),
            P(None, "lag", "space"),
            P("space", None, None),
            P("space", None, None),
            P(),
            P(),
        ),
        out_specs=(P("lag", "space", "member"), P("lag", "space")),
        check_vma=False,
    )
```

```python
import jax
import jax.numpy as jnp
from jax import lax
from jax.sharding import PartitionSpec as P


def spread(array, axis, root):
    mine = lax.axis_index(axis) == root
    return lax.psum(jnp.where(mine, array, jnp.zeros_like(array)), axis)


def innovation(obs_round, values_now, obs_means, errors_now, members):
    highest = lax.Precision.HIGHEST
    obs_total = obs_round.shape[0]
    half = obs_total // 2
    innov_cov = jnp.dot(obs_round, obs_round.T, preferred_element_type=jnp.float32) / (
        members - 1
    ) + jnp.diag(errors_now * errors_now)
    innov_cov = (innov_cov + innov_cov.T) * 0.5
    eye = jnp.eye(half, dtype=jnp.float32)
    eyes = jnp.stack([eye, eye])
    errors_top, errors_low = errors_now[:half], errors_now[half:]
    factor_11 = lax.linalg.cholesky(innov_cov[:half, :half], symmetrize_input=False)
    inv_top = lax.linalg.triangular_solve(
        jnp.stack([factor_11, factor_11 + jnp.diag(errors_top)]), eyes, left_side=True, lower=True
    )
    factor_11_inv, sum_11_inv = inv_top[0], inv_top[1]
    factor_21 = jnp.dot(innov_cov[half:, :half], factor_11_inv.T, precision=highest)
    schur = innov_cov[half:, half:] - jnp.dot(factor_21, factor_21.T, precision=highest)
    factor_22 = lax.linalg.cholesky(schur, symmetrize_input=True)
    inv_low = lax.linalg.triangular_solve(
        jnp.stack([factor_22, factor_22 + jnp.diag(errors_low)]), eyes, left_side=True, lower=True
    )
    factor_22_inv, sum_22_inv = inv_low[0], inv_low[1]
    factor_21_inv = -jnp.dot(
        factor_22_inv, jnp.dot(factor_21, factor_11_inv, precision=highest), precision=highest
    )
    sum_21_inv = -jnp.dot(
        sum_22_inv, jnp.dot(factor_21, sum_11_inv, precision=highest), precision=highest
    )
    zeros = jnp.zeros((half, half), jnp.float32)
    factor_inv = jnp.block([[factor_11_inv, zeros], [factor_21_inv, factor_22_inv]])
    inverse_sum = jnp.block([[sum_11_inv, zeros], [sum_21_inv, sum_22_inv]])
    transform = jnp.dot(factor_inv.T, inverse_sum, precision=highest)
    forward = jnp.dot(factor_inv, values_now - obs_means, precision=highest)
    weights_obs = jnp.dot(factor_inv.T, forward, precision=highest)
    return (transform, weights_obs)


def body(
    anomalies,
    mean_state,
    footprints,
    slot_tiles,
    slot_counts,
    obs_values,
    obs_errors,
    owners,
    batch_order,
):
    highest = lax.Precision.HIGHEST
    high = lax.Precision.HIGH
    batches = footprints.shape[0]
    slot_dev = footprints.shape[2]
    tile_cells = footprints.shape[4]
    member_dev = anomalies.shape[2]
    groups = lax.axis_size("member")
    members = member_dev * groups
    me_member = lax.axis_index("member")
    me_space = lax.axis_index("space")
    me_lag = lax.axis_index("lag")
    lead = (me_member == 0) & (me_lag == 0)
    tile_anoms = anomalies[0].reshape(-1, tile_cells, member_dev)
    tile_means = mean_state[0].reshape(-1, tile_cells)
    tiles_dev = tile_anoms.shape[0]
    all_tiles = lax.all_gather(tile_anoms, "member", axis=2, tiled=True)
    local_ids = jnp.arange(tiles_dev, dtype=jnp.int32)
    slot_place = jnp.arange(slot_dev, dtype=jnp.int32)
    pattern = jnp.zeros((tiles_dev,), jnp.int32)
    pieces, mean_parts, value_parts, error_parts = [], [], [], []
    for position in range(batches):
        batch_now = batch_order[position]
        tile_ids = slot_tiles[batch_now, 0]
        live_slot = slot_place < slot_counts[batch_now, 0, 0]
        prints = footprints[batch_now, 0]
        slot_anoms = tile_anoms[tile_ids]
        slot_means = tile_means[tile_ids].astype(jnp.float32)
        proj = jnp.einsum("spt,stm->spm", prints, slot_anoms, preferred_element_type=jnp.float32)
        n_pat = 2**position
        select = live_slot[:, None] & (
            pattern[tile_ids][:, None] == jnp.arange(n_pat, dtype=jnp.int32)[None, :]
        )
        pieces.append(jnp.sum(jnp.where(select[:, :, None, None], proj[:, None], 0.0), axis=0))
        masked_mean = jnp.where(live_slot[:, None], slot_means, 0.0)
        mean_parts.append(
            jnp.einsum("spt,st->p", prints.astype(jnp.float32), masked_mean, precision=highest)
        )
        owner_here = lead & (me_space == owners[batch_now])
        value_parts.append(jnp.where(owner_here, obs_values[0, batch_now], 0.0))
        error_parts.append(jnp.where(owner_here, obs_errors[0, batch_now], 0.0))
        live_tile = jnp.any((tile_ids[:, None] == local_ids[None, :]) & live_slot[:, None], axis=0)
        pattern = pattern + jnp.where(live_tile, 1 << position, 0)
    projected = jnp.concatenate(pieces, axis=0)
    own_group = (jnp.arange(groups, dtype=jnp.int32) == me_member)[None, :, None, None]
    slotted = jnp.where(own_group, projected[:, None], 0.0)
    mean_parts = jnp.where(me_member == 0, jnp.stack(mean_parts), 0.0)
    summed, obs_means_base, values_all, errors_all = lax.psum(
        (slotted, mean_parts, jnp.stack(value_parts), jnp.stack(error_parts)),
        ("space", "member", "lag"),
    )
    summed = summed.astype(jnp.bfloat16)
    summed = jnp.transpose(summed, (0, 2, 1, 3)).reshape(summed.shape[0], summed.shape[2], members)
    transforms = [jnp.eye(members, dtype=jnp.float32)]
    shifts = [jnp.zeros((members,), jnp.float32)]
    offset = 0
    for position in range(batches):
        n_pat = 2**position
        part = summed[offset : offset + n_pat].astype(jnp.float32)
        offset += n_pat
        obs_anoms = sum(jnp.dot(part[s], t, precision=high) for s, t in enumerate(transforms))
        obs_means = obs_means_base[position] + sum(
            jnp.dot(part[s], v, precision=high) for s, v in enumerate(shifts)
        )
        obs_round = obs_anoms.astype(jnp.bfloat16)
        transform, weights_obs = innovation(
            obs_round, values_all[position], obs_means, errors_all[position], members
        )
        wide_obs = obs_round.astype(jnp.float32)
        step = jnp.dot(
            wide_obs.T, jnp.dot(transform, wide_obs, precision=high), precision=high
        ) / (members - 1)
        lift = jnp.dot(wide_obs.T, weights_obs, precision=high) / (members - 1)
        new_transforms = [t - jnp.dot(t, step, precision=high) for t in transforms]
        new_shifts = [s + jnp.dot(t, lift, precision=high) for t, s in zip(transforms, shifts)]
        transforms = transforms + new_transforms
        shifts = shifts + new_shifts
    own_cols = lax.dynamic_slice_in_dim(
        jnp.stack(transforms), me_member * member_dev, member_dev, axis=2
    )
    tile_transform = own_cols[pattern]
    tile_shift = jnp.stack(shifts)[pattern]
    wide_tiles = all_tiles.astype(jnp.float32)
    updated = jnp.einsum("tcm,tmn->tcn", wide_tiles, tile_transform, precision=high)
    touched = pattern > 0
    new_anoms = jnp.where(touched[:, None, None], updated.astype(jnp.bfloat16), tile_anoms)
    shift_mean = jnp.einsum("tcm,tm->tc", wide_tiles, tile_shift, precision=high)
    new_means = jnp.where(touched[:, None], tile_means + shift_mean, tile_means)
    return (new_anoms.reshape(1, -1, member_dev), new_means.reshape(1, -1))


def solution(mesh):
    return jax.shard_map(
        body,
        mesh=mesh,
        in_specs=(
            P("lag", "space", "member"),
            P("lag", "space"),
            P(None, "lag", "space", None, None),
            P(None, "lag", "space"),
            P(None, "lag", "space"),
            P("space", None, None),
            P("space", None, None),
            P(),
            P(),
        ),
        out_specs=(P("lag", "space", "member"), P("lag", "space")),
        check_vma=False,
    )
```

```python
import jax
import jax.numpy as jnp
from jax import lax
from jax.sharding import PartitionSpec as P


def spread(array, axis, root):
    mine = lax.axis_index(axis) == root
    return lax.psum(jnp.where(mine, array, jnp.zeros_like(array)), axis)


def innovation(obs_round, values_now, obs_means, errors_now, members):
    highest = lax.Precision.HIGHEST
    obs_total = obs_round.shape[0]
    half = obs_total // 2
    innov_cov = jnp.dot(obs_round, obs_round.T, preferred_element_type=jnp.float32) / (
        members - 1
    ) + jnp.diag(errors_now * errors_now)
    innov_cov = (innov_cov + innov_cov.T) * 0.5
    eye = jnp.eye(half, dtype=jnp.float32)
    eyes = jnp.stack([eye, eye])
    errors_top, errors_low = errors_now[:half], errors_now[half:]
    factor_11 = lax.linalg.cholesky(innov_cov[:half, :half], symmetrize_input=False)
    inv_top = lax.linalg.triangular_solve(
        jnp.stack([factor_11, factor_11 + jnp.diag(errors_top)]), eyes, left_side=True, lower=True
    )
    factor_11_inv, sum_11_inv = inv_top[0], inv_top[1]
    factor_21 = jnp.dot(innov_cov[half:, :half], factor_11_inv.T, precision=highest)
    schur = innov_cov[half:, half:] - jnp.dot(factor_21, factor_21.T, precision=highest)
    factor_22 = lax.linalg.cholesky(schur, symmetrize_input=True)
    inv_low = lax.linalg.triangular_solve(
        jnp.stack([factor_22, factor_22 + jnp.diag(errors_low)]), eyes, left_side=True, lower=True
    )
    factor_22_inv, sum_22_inv = inv_low[0], inv_low[1]
    factor_21_inv = -jnp.dot(
        factor_22_inv, jnp.dot(factor_21, factor_11_inv, precision=highest), precision=highest
    )
    sum_21_inv = -jnp.dot(
        sum_22_inv, jnp.dot(factor_21, sum_11_inv, precision=highest), precision=highest
    )
    zeros = jnp.zeros((half, half), jnp.float32)
    factor_inv = jnp.block([[factor_11_inv, zeros], [factor_21_inv, factor_22_inv]])
    inverse_sum = jnp.block([[sum_11_inv, zeros], [sum_21_inv, sum_22_inv]])
    transform = jnp.dot(factor_inv.T, inverse_sum, precision=highest)
    forward = jnp.dot(factor_inv, values_now - obs_means, precision=highest)
    weights_obs = jnp.dot(factor_inv.T, forward, precision=highest)
    return (transform, weights_obs)


def body(
    anomalies,
    mean_state,
    footprints,
    slot_tiles,
    slot_counts,
    obs_values,
    obs_errors,
    owners,
    batch_order,
):
    highest = lax.Precision.HIGHEST
    high = lax.Precision.HIGH
    batches = footprints.shape[0]
    slot_dev = footprints.shape[2]
    tile_cells = footprints.shape[4]
    member_dev = anomalies.shape[2]
    groups = lax.axis_size("member")
    members = member_dev * groups
    me_member = lax.axis_index("member")
    me_space = lax.axis_index("space")
    me_lag = lax.axis_index("lag")
    lead = (me_member == 0) & (me_lag == 0)
    tile_anoms = anomalies[0].reshape(-1, tile_cells, member_dev)
    tile_means = mean_state[0].reshape(-1, tile_cells)
    tiles_dev = tile_anoms.shape[0]
    all_tiles = lax.all_gather(tile_anoms, "member", axis=2, tiled=True)
    local_ids = jnp.arange(tiles_dev, dtype=jnp.int32)
    slot_place = jnp.arange(slot_dev, dtype=jnp.int32)
    pattern = jnp.zeros((tiles_dev,), jnp.int32)
    pieces, mean_parts, value_parts, error_parts = [], [], [], []
    for position in range(batches):
        batch_now = batch_order[position]
        tile_ids = slot_tiles[batch_now, 0]
        live_slot = slot_place < slot_counts[batch_now, 0, 0]
        prints = footprints[batch_now, 0]
        slot_anoms = tile_anoms[tile_ids]
        slot_means = tile_means[tile_ids].astype(jnp.float32)
        proj = jnp.einsum("spt,stm->spm", prints, slot_anoms, preferred_element_type=jnp.float32)
        n_pat = 2**position
        select = live_slot[:, None] & (
            pattern[tile_ids][:, None] == jnp.arange(n_pat, dtype=jnp.int32)[None, :]
        )
        pieces.append(jnp.sum(jnp.where(select[:, :, None, None], proj[:, None], 0.0), axis=0))
        masked_mean = jnp.where(live_slot[:, None], slot_means, 0.0)
        mean_parts.append(
            jnp.einsum("spt,st->p", prints.astype(jnp.float32), masked_mean, precision=highest)
        )
        owner_here = lead & (me_space == owners[batch_now])
        value_parts.append(jnp.where(owner_here, obs_values[0, batch_now], 0.0))
        error_parts.append(jnp.where(owner_here, obs_errors[0, batch_now], 0.0))
        live_tile = jnp.any((tile_ids[:, None] == local_ids[None, :]) & live_slot[:, None], axis=0)
        pattern = pattern + jnp.where(live_tile, 1 << position, 0)
    projected = jnp.concatenate(pieces, axis=0)
    own_group = (jnp.arange(groups, dtype=jnp.int32) == me_member)[None, :, None, None]
    slotted = jnp.where(own_group, projected[:, None], 0.0)
    mean_parts = jnp.where(me_member == 0, jnp.stack(mean_parts), 0.0)
    summed, obs_means_base, values_all, errors_all = lax.psum(
        (slotted, mean_parts, jnp.stack(value_parts), jnp.stack(error_parts)),
        ("space", "member", "lag"),
    )
    summed = summed.astype(jnp.bfloat16)
    summed = jnp.transpose(summed, (0, 2, 1, 3)).reshape(summed.shape[0], summed.shape[2], members)
    transforms = [jnp.eye(members, dtype=jnp.float32)]
    shifts = [jnp.zeros((members,), jnp.float32)]
    offset = 0
    for position in range(batches):
        n_pat = 2**position
        part = summed[offset : offset + n_pat].astype(jnp.float32)
        offset += n_pat
        if position == 0:
            obs_anoms = part[0]
            obs_means = obs_means_base[position]
        else:
            obs_anoms = sum(jnp.dot(part[s], t, precision=high) for s, t in enumerate(transforms))
            obs_means = obs_means_base[position] + sum(
                jnp.dot(part[s], v, precision=high) for s, v in enumerate(shifts)
            )
        obs_round = obs_anoms.astype(jnp.bfloat16)
        transform, weights_obs = innovation(
            obs_round, values_all[position], obs_means, errors_all[position], members
        )
        wide_obs = obs_round.astype(jnp.float32)
        step = jnp.dot(
            wide_obs.T, jnp.dot(transform, wide_obs, precision=high), precision=high
        ) / (members - 1)
        lift = jnp.dot(wide_obs.T, weights_obs, precision=high) / (members - 1)
        if position == batches - 1:
            own_step = lax.dynamic_slice_in_dim(step, me_member * member_dev, member_dev, axis=1)
            own_cols = [
                lax.dynamic_slice_in_dim(t, me_member * member_dev, member_dev, axis=1)
                for t in transforms
            ]
            own_cols = own_cols + [
                c - jnp.dot(t, own_step, precision=high) for t, c in zip(transforms, own_cols)
            ]
        elif position == 0:
            transforms = transforms + [transforms[0] - step]
        else:
            transforms = transforms + [t - jnp.dot(t, step, precision=high) for t in transforms]
        if position == 0:
            shifts = shifts + [lift]
        else:
            shifts = shifts + [s + jnp.dot(t, lift, precision=high) for t, s in zip(transforms, shifts)]
    own_cols = jnp.stack(own_cols)
    tile_transform = own_cols[pattern]
    tile_shift = jnp.stack(shifts)[pattern]
    wide_tiles = all_tiles.astype(jnp.float32)
    updated = jnp.einsum("tcm,tmn->tcn", wide_tiles, tile_transform, precision=high)
    touched = pattern > 0
    new_anoms = jnp.where(touched[:, None, None], updated.astype(jnp.bfloat16), tile_anoms)
    shift_mean = jnp.einsum("tcm,tm->tc", wide_tiles, tile_shift, precision=high)
    new_means = jnp.where(touched[:, None], tile_means + shift_mean, tile_means)
    return (new_anoms.reshape(1, -1, member_dev), new_means.reshape(1, -1))


def solution(mesh):
    return jax.shard_map(
        body,
        mesh=mesh,
        in_specs=(
            P("lag", "space", "member"),
            P("lag", "space"),
            P(None, "lag", "space", None, None),
            P(None, "lag", "space"),
            P(None, "lag", "space"),
            P("space", None, None),
            P("space", None, None),
            P(),
            P(),
        ),
        out_specs=(P("lag", "space", "member"), P("lag", "space")),
        check_vma=False,
    )
```

```python
import jax
import jax.numpy as jnp
from jax import lax
from jax.sharding import PartitionSpec as P


def spread(array, axis, root):
    mine = lax.axis_index(axis) == root
    return lax.psum(jnp.where(mine, array, jnp.zeros_like(array)), axis)


def innovation(obs_round, values_now, obs_means, errors_now, members):
    highest = lax.Precision.HIGHEST
    obs_total = obs_round.shape[0]
    half = obs_total // 2
    innov_cov = jnp.dot(obs_round, obs_round.T, preferred_element_type=jnp.float32) / (
        members - 1
    ) + jnp.diag(errors_now * errors_now)
    innov_cov = (innov_cov + innov_cov.T) * 0.5
    eye = jnp.eye(half, dtype=jnp.float32)
    eyes = jnp.stack([eye, eye])
    errors_top, errors_low = errors_now[:half], errors_now[half:]
    factor_11 = lax.linalg.cholesky(innov_cov[:half, :half], symmetrize_input=False)
    inv_top = lax.linalg.triangular_solve(
        jnp.stack([factor_11, factor_11 + jnp.diag(errors_top)]), eyes, left_side=True, lower=True
    )
    factor_11_inv, sum_11_inv = inv_top[0], inv_top[1]
    factor_21 = jnp.dot(innov_cov[half:, :half], factor_11_inv.T, precision=highest)
    schur = innov_cov[half:, half:] - jnp.dot(factor_21, factor_21.T, precision=highest)
    factor_22 = lax.linalg.cholesky(schur, symmetrize_input=True)
    inv_low = lax.linalg.triangular_solve(
        jnp.stack([factor_22, factor_22 + jnp.diag(errors_low)]), eyes, left_side=True, lower=True
    )
    factor_22_inv, sum_22_inv = inv_low[0], inv_low[1]
    factor_21_inv = -jnp.dot(
        factor_22_inv, jnp.dot(factor_21, factor_11_inv, precision=highest), precision=highest
    )
    sum_21_inv = -jnp.dot(
        sum_22_inv, jnp.dot(factor_21, sum_11_inv, precision=highest), precision=highest
    )
    zeros = jnp.zeros((half, half), jnp.float32)
    factor_inv = jnp.block([[factor_11_inv, zeros], [factor_21_inv, factor_22_inv]])
    inverse_sum = jnp.block([[sum_11_inv, zeros], [sum_21_inv, sum_22_inv]])
    transform = jnp.dot(factor_inv.T, inverse_sum, precision=highest)
    forward = jnp.dot(factor_inv, values_now - obs_means, precision=highest)
    weights_obs = jnp.dot(factor_inv.T, forward, precision=highest)
    return (transform, weights_obs)


def body(
    anomalies,
    mean_state,
    footprints,
    slot_tiles,
    slot_counts,
    obs_values,
    obs_errors,
    owners,
    batch_order,
):
    highest = lax.Precision.HIGHEST
    high = lax.Precision.HIGH
    batches = footprints.shape[0]
    slot_dev = footprints.shape[2]
    tile_cells = footprints.shape[4]
    member_dev = anomalies.shape[2]
    groups = lax.axis_size("member")
    members = member_dev * groups
    me_member = lax.axis_index("member")
    me_space = lax.axis_index("space")
    me_lag = lax.axis_index("lag")
    lead = (me_member == 0) & (me_lag == 0)
    tile_anoms = anomalies[0].reshape(-1, tile_cells, member_dev)
    tile_means = mean_state[0].reshape(-1, tile_cells)
    tiles_dev = tile_anoms.shape[0]
    all_tiles = lax.all_gather(tile_anoms, "member", axis=2, tiled=True)
    local_ids = jnp.arange(tiles_dev, dtype=jnp.int32)
    slot_place = jnp.arange(slot_dev, dtype=jnp.int32)
    pattern = jnp.zeros((tiles_dev,), jnp.int32)
    pieces, mean_parts, value_parts, error_parts = [], [], [], []
    for position in range(batches):
        batch_now = batch_order[position]
        tile_ids = slot_tiles[batch_now, 0]
        live_slot = slot_place < slot_counts[batch_now, 0, 0]
        prints = footprints[batch_now, 0]
        slot_anoms = tile_anoms[tile_ids]
        slot_means = tile_means[tile_ids].astype(jnp.float32)
        proj = jnp.einsum("spt,stm->spm", prints, slot_anoms, preferred_element_type=jnp.float32)
        n_pat = 2**position
        select = live_slot[:, None] & (
            pattern[tile_ids][:, None] == jnp.arange(n_pat, dtype=jnp.int32)[None, :]
        )
        pieces.append(jnp.sum(jnp.where(select[:, :, None, None], proj[:, None], 0.0), axis=0))
        masked_mean = jnp.where(live_slot[:, None], slot_means, 0.0)
        mean_parts.append(
            jnp.einsum("spt,st->p", prints.astype(jnp.float32), masked_mean, precision=highest)
        )
        owner_here = lead & (me_space == owners[batch_now])
        value_parts.append(jnp.where(owner_here, obs_values[0, batch_now], 0.0))
        error_parts.append(jnp.where(owner_here, obs_errors[0, batch_now], 0.0))
        live_tile = jnp.any((tile_ids[:, None] == local_ids[None, :]) & live_slot[:, None], axis=0)
        pattern = pattern + jnp.where(live_tile, 1 << position, 0)
    projected = jnp.concatenate(pieces, axis=0)
    own_group = (jnp.arange(groups, dtype=jnp.int32) == me_member)[None, :, None, None]
    slotted = jnp.where(own_group, projected[:, None], 0.0)
    mean_parts = jnp.where(me_member == 0, jnp.stack(mean_parts), 0.0)
    summed, obs_means_base, values_all, errors_all = lax.psum(
        (slotted, mean_parts, jnp.stack(value_parts), jnp.stack(error_parts)),
        ("space", "member", "lag"),
    )
    summed = summed.astype(jnp.bfloat16)
    summed = jnp.transpose(summed, (0, 2, 1, 3)).reshape(summed.shape[0], summed.shape[2], members)
    transforms = [jnp.eye(members, dtype=jnp.float32)]
    shifts = [jnp.zeros((members,), jnp.float32)]
    offset = 0
    for position in range(batches):
        n_pat = 2**position
        part = summed[offset : offset + n_pat].astype(jnp.float32)
        offset += n_pat
        if position == 0:
            obs_anoms = part[0]
            obs_means = obs_means_base[position]
        else:
            obs_anoms = sum(jnp.dot(part[s], t, precision=high) for s, t in enumerate(transforms))
            obs_means = obs_means_base[position] + sum(
                jnp.dot(part[s], v, precision=high) for s, v in enumerate(shifts)
            )
        obs_round = obs_anoms.astype(jnp.bfloat16)
        transform, weights_obs = innovation(
            obs_round, values_all[position], obs_means, errors_all[position], members
        )
        wide_obs = obs_round.astype(jnp.float32)
        step = jnp.dot(
            wide_obs.T, jnp.dot(transform, wide_obs, precision=high), precision=high
        ) / (members - 1)
        lift = jnp.dot(wide_obs.T, weights_obs, precision=high) / (members - 1)
        new_transforms = [t - jnp.dot(t, step, precision=high) for t in transforms]
        new_shifts = [s + jnp.dot(t, lift, precision=high) for t, s in zip(transforms, shifts)]
        transforms = transforms + new_transforms
        shifts = shifts + new_shifts
    own_cols = lax.dynamic_slice_in_dim(
        jnp.stack(transforms), me_member * member_dev, member_dev, axis=2
    )
    tile_transform = own_cols[pattern]
    tile_shift = jnp.stack(shifts)[pattern]
    wide_tiles = all_tiles.astype(jnp.float32)
    updated = jnp.einsum("tcm,tmn->tcn", wide_tiles, tile_transform, precision=high)
    touched = pattern > 0
    new_anoms = jnp.where(touched[:, None, None], updated.astype(jnp.bfloat16), tile_anoms)
    shift_mean = jnp.einsum("tcm,tm->tc", wide_tiles, tile_shift, precision=high)
    new_means = jnp.where(touched[:, None], tile_means + shift_mean, tile_means)
    return (new_anoms.reshape(1, -1, member_dev), new_means.reshape(1, -1))


def solution(mesh):
    return jax.shard_map(
        body,
        mesh=mesh,
        in_specs=(
            P("lag", "space", "member"),
            P("lag", "space"),
            P(None, "lag", "space", None, None),
            P(None, "lag", "space"),
            P(None, "lag", "space"),
            P("space", None, None),
            P("space", None, None),
            P(),
            P(),
        ),
        out_specs=(P("lag", "space", "member"), P("lag", "space")),
        check_vma=False,
    )
```
